256 devices in a mesh: uly: 16 (over y, x), blk: 16 (over z, core).
Axes of the slice: x: 4, y: 4, z: 8, core: 2. Of those that a mesh axis runs over, the one named last changes fastest.
Arguments:
- query_rows: bfloat16 [98304, 2048], P(('uly', 'blk')), may hold values from -8 to 8
- key_rows: bfloat16 [98304, 2048], P(('uly', 'blk')), may hold values from -8 to 8
- value_rows: bfloat16 [98304, 2048], P(('uly', 'blk')), may hold values from -6 to 6
- kept_tiles: int32 [256, 6], replicated, may hold values from -1 to 255, as said below
Outputs:
- attended: bfloat16 [98304, 2048], P(('uly', 'blk'))
The draws below stay inside these ranges and needn't reach their ends.
Inputs may be any that keep to these rules, and one draw needn't show every extreme that they name: `kept_tiles`: tile t = p * 16 + a with p = b * 4 + c has coordinates (b, a, c) with 0 <= b < 4, 0 <= a < 16, 0 <= c < 4; slab a is the tiles with that a, and p is a tile's position in its slab. Row t lists distinct tiles, t itself first, then the others, then -1 in the unused entries; every listed tile differs from t by at most 1 in each coordinate. For every slab a and each of the slabs a - 1 and a + 1, the tiles of that neighbouring slab listed by queries of slab a lie within 8 consecutive positions. Some row fills all 6 entries.
All inputs are finite; a program needn't handle non-finite values.
Results may differ from the reference program's by a relative error of at most 0.0047.
Values may be sent and summed in bfloat16 or wider, within the bound.
No kernel may reach another device: no remote copies, remote signals or barrier semaphores. Data moves between devices by JAX's collectives and lax.ppermute only.
A program may use at most 64 MiB of HBM per device.

```python
import jax
import jax.numpy as jnp
from jax import lax

HEAD_DIM = 128
TILE = 384
KEEP = 6
TC = 4
HEADS = 16
TA = 16
TB = 4
SLAB = 16
USED = 8
TILES = 256
TOKENS = 98304


def normal_base(key):
    return jnp.clip(jax.random.normal(key, (TOKENS, HEADS * HEAD_DIM), jnp.float32), -6.0, 6.0)


def draw_query_rows(key, part):
    result = normal_base(jax.random.fold_in(key, 5))
    return result.astype(jnp.bfloat16)


def draw_key_rows(key, part):
    result = normal_base(jax.random.fold_in(key, 6))
    return result.astype(jnp.bfloat16)


def draw_kept_tiles(key, part):
    run_starts = jax.random.randint(jax.random.fold_in(key, 11), (TA, 2), 0, SLAB - USED + 1)
    tile_ids = jnp.arange(TILES, dtype=jnp.int32)
    coord_a = tile_ids % TA
    slab_pos = tile_ids // TA
    coord_b = slab_pos // TC
    coord_c = slab_pos % TC
    offset_ids = jnp.arange(27, dtype=jnp.int32)
    shift_b = offset_ids // 9 - 1
    shift_a = offset_ids // 3 % 3 - 1
    shift_c = offset_ids % 3 - 1
    key_b = coord_b[:, None] + shift_b[None, :]
    key_a = coord_a[:, None] + shift_a[None, :]
    key_c = coord_c[:, None] + shift_c[None, :]
    inside = (key_b >= 0) & (key_b < TB) & (key_a >= 0) & (key_a < TA) & (key_c >= 0) & (key_c < TC)
    position = key_b * TC + key_c
    side_index = jnp.where(shift_a > 0, 1, 0)
    run_low = run_starts[coord_a[:, None], side_index[None, :]]
    in_run = (position >= run_low) & (position < run_low + USED)
    allowed = inside & ((shift_a == 0)[None, :] | in_run)
    own_offset = (shift_a == 0) & (shift_b == 0) & (shift_c == 0)
    direct = (shift_a != 0) & (shift_b == 0) & (shift_c == 0)
    forced = allowed & direct[None, :]
    level = jnp.where(own_offset[None, :], 3, jnp.where(forced, 2, jnp.where(allowed, 1, 0)))
    noise = jax.random.randint(jax.random.fold_in(key, 12), (TILES, 27), 0, 1 << 20)
    ranking = level * (1 << 26) + noise * 32 + jnp.arange(27, dtype=jnp.int32)[None, :]
    ranked, chosen = lax.top_k(ranking, KEEP)
    count_live = jnp.sum(allowed.astype(jnp.int32), axis=1)
    count_forced = jnp.sum((level >= 2).astype(jnp.int32), axis=1)
    wanted = jax.random.randint(jax.random.fold_in(key, 13), (TILES,), 3, KEEP + 1)
    wanted = jnp.where(tile_ids % 4 == 0, KEEP, wanted)
    chosen_pos = run_starts[1, 1] + USED // 2
    chosen_tile = chosen_pos * TA + 1
    wanted = jnp.where(tile_ids == chosen_tile, KEEP, wanted)
    live_count = jnp.minimum(jnp.maximum(wanted, count_forced), count_live)
    key_tile = (key_b * TC + key_c) * TA + key_a
    picked = jnp.take_along_axis(key_tile, chosen, axis=1)
    slot_index = jnp.arange(KEEP, dtype=jnp.int32)
    return jnp.where(slot_index[None, :] < live_count[:, None], picked, -1).astype(jnp.int32)


def shard_levels(rng, extent, pieces, low, largest):
    loudness, own = 1.0, jax.random.fold_in(rng, 6)
    for axis_at, blocks in pieces:
        heights = jnp.exp(jax.random.uniform(jax.random.fold_in(own, axis_at), (blocks,), jnp.float32, low / len(pieces), largest / len(pieces)))
        loudness = loudness * jnp.repeat(heights, extent[axis_at] // blocks).reshape([-1 if axis == axis_at else 1 for axis in range(len(extent))])
    return loudness


def bell_draw(own_key, shape, scale, bound, pieces=(), held_as=jnp.bfloat16):
    drawn = jax.random.normal(own_key, shape, jnp.float32) * scale
    if len(pieces) > 0:
        drawn = shard_levels(own_key, shape, pieces, -0.22, 0.18) * drawn
    return jnp.clip(drawn, min=-bound, max=bound).astype(held_as)


def setup_inputs(seed: int = 0) -> dict:
    seeds = jax.random.split(jax.random.key(seed), 5)
    query_rows = draw_query_rows(jax.random.fold_in(seeds[4], 71), 0)
    key_rows = draw_key_rows(jax.random.fold_in(seeds[4], 71), 0)
    value_rows = bell_draw(seeds[2], (TOKENS, HEADS * HEAD_DIM), 1.0, 6.0, ((0, 256),))
    kept_tiles = draw_kept_tiles(jax.random.fold_in(seeds[4], 71), 0)
    return dict(query_rows=query_rows, key_rows=key_rows, value_rows=value_rows, kept_tiles=kept_tiles)


def reference(query_rows, key_rows, value_rows, kept_tiles):
    score_scale = HEAD_DIM ** -0.5
    query_tiles = query_rows.reshape(TILES, TILE, HEADS, HEAD_DIM)
    key_tiles = key_rows.reshape(TILES, TILE, HEADS, HEAD_DIM)
    value_tiles = value_rows.reshape(TILES, TILE, HEADS, HEAD_DIM)

    def attend_tile(tile_id):
        listed = kept_tiles[tile_id]
        is_live = listed >= 0
        safe_ids = jnp.where(is_live, listed, 0).astype(jnp.int32)
        key_gather = key_tiles[safe_ids].astype(jnp.float32)
        value_gather = value_tiles[safe_ids].astype(jnp.float32)
        query_block = query_tiles[tile_id].astype(jnp.float32)
        scores = jnp.einsum("ihd,kjhd->hikj", query_block, key_gather) * score_scale
        scores = jnp.where(is_live[None, None, :, None], scores, -jnp.inf)
        row_max = jnp.max(scores, axis=(2, 3), keepdims=True)
        weights = jnp.exp(scores - row_max)
        totals = jnp.sum(weights, axis=(2, 3))
        weights_low = lax.optimization_barrier(weights.astype(jnp.bfloat16)).astype(jnp.float32)
        mixed = jnp.einsum("hikj,kjhd->ihd", weights_low, value_gather)
        mixed = mixed / jnp.transpose(totals)[:, :, None]
        return mixed.astype(jnp.bfloat16)

    attended = lax.map(attend_tile, jnp.arange(TILES, dtype=jnp.int32))
    return attended.reshape(TOKENS, HEADS * HEAD_DIM)
```

```python
import functools

import jax
import jax.numpy as jnp
from jax import lax
from jax.experimental import pallas as pl
from jax.experimental.pallas import tpu as pltpu
from jax.sharding import PartitionSpec as P

HEAD_DIM = 128
TILE = 384
KEEP = 6
USED = 8


def passed_along(block, axis, distance):
    devices = range(lax.axis_size(axis))
    route = [(i - distance, i) for i in devices if i - distance in devices]
    return lax.ppermute(block, axis, route)


def run_starts(kept_tiles, n_blk, slab_tiles):
    rows = kept_tiles.shape[0]
    row_slab = (jnp.arange(rows, dtype=jnp.int32) % n_blk)[:, None]
    live = kept_tiles >= 0
    entry_slab = jnp.where(live, kept_tiles % n_blk, -5)
    entry_pos = kept_tiles // n_blk
    slabs = jnp.arange(n_blk, dtype=jnp.int32)
    big = jnp.int32(slab_tiles + 1)

    def start_for(shift):
        hit = (row_slab[None] == slabs[:, None, None]) & (
            entry_slab[None] == slabs[:, None, None] + shift
        )
        low = jnp.min(jnp.where(hit, entry_pos[None], big), axis=(1, 2))
        return jnp.where(low == big, 0, jnp.minimum(low, slab_tiles - USED))

    return start_for(-1), start_for(1)


def attend_kernel(which_ref, index_ref, count_ref, q_ref, kl_ref, kc_ref, kr_ref,
                  vl_ref, vc_ref, vr_ref, o_ref, s_scr, m_scr, l_scr, acc_scr):
    i = pl.program_id(0)
    n = count_ref[i]
    score_scale = HEAD_DIM ** (-0.5)
    q = q_ref[0]

    def pick(l_ref, c_ref, r_ref, j):
        w = which_ref[i * KEEP + j]
        x = index_ref[i * KEEP + j]
        side = l_ref.shape[0] - 1
        own = c_ref.shape[0] - 1
        a = l_ref[jnp.clip(x, 0, side)]
        b = c_ref[jnp.clip(x, 0, own)]
        c = r_ref[jnp.clip(x, 0, side)]
        return jnp.where(w == 0, a, jnp.where(w == 1, b, c))

    for j in range(KEEP):
        @pl.when(j < n)
        def _():
            k = pick(kl_ref, kc_ref, kr_ref, j)
            s = lax.dot_general(q, k, (((1,), (1,)), ((), ())),
                                preferred_element_type=jnp.float32) * score_scale
            s_scr[j] = s
            mj = jnp.max(s, axis=1, keepdims=True)
            if j == 0:
                m_scr[...] = mj
            else:
                m_scr[...] = jnp.maximum(m_scr[...], mj)

    m = m_scr[...]
    for j in range(KEEP):
        @pl.when(j < n)
        def _():
            p = jnp.exp(s_scr[j] - m)
            lsum = jnp.sum(p, axis=1, keepdims=True)
            v = pick(vl_ref, vc_ref, vr_ref, j)
            pv = jnp.dot(p.astype(jnp.bfloat16), v, preferred_element_type=jnp.float32)
            if j == 0:
                l_scr[...] = lsum
                acc_scr[...] = pv
            else:
                l_scr[...] = l_scr[...] + lsum
                acc_scr[...] = acc_scr[...] + pv

    o_ref[0] = (acc_scr[...] / l_scr[...]).astype(o_ref.dtype)


def attend(which, index, count, q, kl, kc, kr, vl, vc, vr):
    n_q, tile, width = q.shape
    side = kl.shape[0]
    own = kc.shape[0]
    whole_side = pl.BlockSpec((side, tile, width), lambda i, *_: (0, 0, 0))
    whole_own = pl.BlockSpec((own, tile, width), lambda i, *_: (0, 0, 0))
    one = pl.BlockSpec((1, tile, width), lambda i, *_: (i, 0, 0))
    grid_spec = pltpu.PrefetchScalarGridSpec(
        num_scalar_prefetch=3,
        grid=(n_q,),
        in_specs=[one, whole_side, whole_own, whole_side, whole_side, whole_own, whole_side],
        out_specs=one,
        scratch_shapes=[
            pltpu.VMEM((KEEP, tile, tile), jnp.float32),
            pltpu.VMEM((tile, 1), jnp.float32),
            pltpu.VMEM((tile, 1), jnp.float32),
            pltpu.VMEM((tile, width), jnp.float32),
        ],
    )
    flops = n_q * KEEP * tile * tile * width * 4
    cost = pl.CostEstimate(
        flops=flops,
        transcendentals=n_q * KEEP * tile * tile,
        bytes_accessed=2 * (q.size * 2 + (kl.size + kc.size + kr.size) * 2),
    )
    return pl.pallas_call(
        attend_kernel,
        grid_spec=grid_spec,
        out_shape=jax.ShapeDtypeStruct(q.shape, q.dtype),
        compiler_params=pltpu.CompilerParams(dimension_semantics=("arbitrary",)),
        cost_estimate=cost,
    )(which, index, count, q, kl, kc, kr, vl, vc, vr)


def body(query_rows, key_rows, value_rows, kept_tiles):
    query_local, key_local, value_local = (
        lax.all_to_all(query_rows, "uly", split_axis=1, concat_axis=0, tiled=True),
        lax.all_to_all(key_rows, "uly", split_axis=1, concat_axis=0, tiled=True),
        lax.all_to_all(value_rows, "uly", split_axis=1, concat_axis=0, tiled=True),
    )
    n_uly = lax.axis_size("uly")
    n_blk = lax.axis_size("blk")
    feat_width = query_local.shape[1]
    slab_now = lax.axis_index("blk")

    from_left, from_right = run_starts(kept_tiles, n_blk, n_uly)
    key_tiles = key_local.reshape(n_uly, TILE, feat_width)
    value_tiles = value_local.reshape(n_uly, TILE, feat_width)
    query_tiles = query_local.reshape(n_uly, TILE, feat_width)

    to_next = from_left[jnp.minimum(slab_now + 1, n_blk - 1)]
    to_prev = from_right[jnp.maximum(slab_now - 1, 0)]
    run_next = (
        lax.dynamic_slice_in_dim(key_tiles, to_next, USED, 0),
        lax.dynamic_slice_in_dim(value_tiles, to_next, USED, 0),
    )
    run_prev = (
        lax.dynamic_slice_in_dim(key_tiles, to_prev, USED, 0),
        lax.dynamic_slice_in_dim(value_tiles, to_prev, USED, 0),
    )
    left_key, left_value = passed_along(run_next, "blk", 1)
    right_key, right_value = passed_along(run_prev, "blk", -1)

    position = jnp.arange(n_uly, dtype=jnp.int32)
    listed = jnp.take(kept_tiles, position * n_blk + slab_now, axis=0)
    is_live = listed >= 0
    safe = jnp.where(is_live, listed, 0)
    relative = safe % n_blk - slab_now
    tile_pos = safe // n_blk
    which = (relative + 1).astype(jnp.int32)
    index = jnp.where(
        relative == 0,
        tile_pos,
        jnp.where(relative < 0, tile_pos - from_left[slab_now], tile_pos - from_right[slab_now]),
    ).astype(jnp.int32)
    index = jnp.where(is_live, index, 0)
    which = jnp.where(is_live, which, 1)
    count = jnp.sum(is_live.astype(jnp.int32), axis=1)

    attended = attend(
        which.reshape(-1), index.reshape(-1), count,
        query_tiles, left_key, key_tiles, right_key, left_value, value_tiles, right_value,
    )
    attended = attended.reshape(n_uly * TILE, feat_width)
    return lax.all_to_all(attended, "uly", split_axis=0, concat_axis=1, tiled=True)


def solution(mesh):
    placed = (P(("uly", "blk"), None), P(("uly", "blk"), None), P(("uly", "blk"), None), P())
    return jax.shard_map(
        body, mesh=mesh, in_specs=placed, out_specs=P(("uly", "blk"), None), check_vma=False
    )
```

```python
import functools

import jax
import jax.numpy as jnp
from jax import lax
from jax.experimental import pallas as pl
from jax.experimental.pallas import tpu as pltpu
from jax.sharding import PartitionSpec as P

HEAD_DIM = 128
TILE = 384
KEEP = 6
USED = 8
CHUNKS = 2
LOG2_E = 1.4426950408889634


def passed_along(block, axis, distance):
    devices = range(lax.axis_size(axis))
    route = [(i - distance, i) for i in devices if i - distance in devices]
    return lax.ppermute(block, axis, route)


def run_starts(kept_tiles, n_blk, slab_tiles):
    rows = kept_tiles.shape[0]
    row_slab = (jnp.arange(rows, dtype=jnp.int32) % n_blk)[:, None]
    live = kept_tiles >= 0
    entry_slab = jnp.where(live, kept_tiles % n_blk, -5)
    entry_pos = kept_tiles // n_blk
    slabs = jnp.arange(n_blk, dtype=jnp.int32)
    big = jnp.int32(slab_tiles + 1)

    def start_for(shift):
        hit = (row_slab[None] == slabs[:, None, None]) & (
            entry_slab[None] == slabs[:, None, None] + shift
        )
        low = jnp.min(jnp.where(hit, entry_pos[None], big), axis=(1, 2))
        return jnp.where(low == big, 0, jnp.minimum(low, slab_tiles - USED))

    return start_for(-1), start_for(1)


def attend_kernel(which_ref, index_ref, count_ref, q_ref, kl_ref, kc_ref, kr_ref,
                  vl_ref, vc_ref, vr_ref, o_ref, s_scr, mx_scr, lacc_scr, acc_scr):
    i = pl.program_id(0)
    n = count_ref[i]
    score_scale = (HEAD_DIM ** (-0.5)) * LOG2_E
    q = q_ref[0]

    def pick(l_ref, c_ref, r_ref, j):
        w = which_ref[i * KEEP + j]
        x = index_ref[i * KEEP + j]
        side = l_ref.shape[0] - 1
        own = c_ref.shape[0] - 1
        a = l_ref[jnp.clip(x, 0, side)]
        b = c_ref[jnp.clip(x, 0, own)]
        c = r_ref[jnp.clip(x, 0, side)]
        return jnp.where(w == 0, a, jnp.where(w == 1, b, c))

    for j in range(KEEP):
        @pl.when(j < n)
        def _():
            k = pick(kl_ref, kc_ref, kr_ref, j)
            s = lax.dot_general(q, k, (((1,), (1,)), ((), ())),
                                preferred_element_type=jnp.float32) * score_scale
            s_scr[j] = s
            if j == 0:
                mx_scr[...] = s
            else:
                mx_scr[...] = jnp.maximum(mx_scr[...], s)

    m = jnp.max(mx_scr[...], axis=1, keepdims=True)
    for j in range(KEEP):
        @pl.when(j < n)
        def _():
            p = jnp.exp2(s_scr[j] - m)
            v = pick(vl_ref, vc_ref, vr_ref, j)
            pv = jnp.dot(p.astype(jnp.bfloat16), v, preferred_element_type=jnp.float32)
            if j == 0:
                lacc_scr[...] = p
                acc_scr[...] = pv
            else:
                lacc_scr[...] = lacc_scr[...] + p
                acc_scr[...] = acc_scr[...] + pv

    total = jnp.sum(lacc_scr[...], axis=1, keepdims=True)
    o_ref[0] = (acc_scr[...] / total).astype(o_ref.dtype)


def attend(which, index, count, q, kl, kc, kr, vl, vc, vr):
    n_q, tile, width = q.shape
    side = kl.shape[0]
    own = kc.shape[0]
    key_tile = kc.shape[1]
    whole_side = pl.BlockSpec((side, key_tile, width), lambda i, *_: (0, 0, 0))
    whole_own = pl.BlockSpec((own, key_tile, width), lambda i, *_: (0, 0, 0))
    one = pl.BlockSpec((1, tile, width), lambda i, *_: (i, 0, 0))
    grid_spec = pltpu.PrefetchScalarGridSpec(
        num_scalar_prefetch=3,
        grid=(n_q,),
        in_specs=[one, whole_side, whole_own, whole_side, whole_side, whole_own, whole_side],
        out_specs=one,
        scratch_shapes=[
            pltpu.VMEM((KEEP, tile, key_tile), jnp.float32),
            pltpu.VMEM((tile, key_tile), jnp.float32),
            pltpu.VMEM((tile, key_tile), jnp.float32),
            pltpu.VMEM((tile, width), jnp.float32),
        ],
    )
    flops = n_q * KEEP * tile * key_tile * width * 4
    cost = pl.CostEstimate(
        flops=flops,
        transcendentals=n_q * KEEP * tile * key_tile,
        bytes_accessed=2 * (q.size * 2 + (kl.size + kc.size + kr.size) * 2),
    )
    return pl.pallas_call(
        attend_kernel,
        grid_spec=grid_spec,
        out_shape=jax.ShapeDtypeStruct(q.shape, q.dtype),
        compiler_params=pltpu.CompilerParams(dimension_semantics=("arbitrary",)),
        cost_estimate=cost,
    )(which, index, count, q, kl, kc, kr, vl, vc, vr)


def body(query_rows, key_rows, value_rows, kept_tiles):
    key_local, value_local = (
        lax.all_to_all(key_rows, "uly", split_axis=1, concat_axis=0, tiled=True),
        lax.all_to_all(value_rows, "uly", split_axis=1, concat_axis=0, tiled=True),
    )
    n_uly = lax.axis_size("uly")
    n_blk = lax.axis_size("blk")
    feat_width = key_local.shape[1]
    slab_now = lax.axis_index("blk")
    rows = query_rows.shape[0]
    chunk = rows // CHUNKS

    from_left, from_right = run_starts(kept_tiles, n_blk, n_uly)
    key_tiles = key_local.reshape(n_uly, TILE, feat_width)
    value_tiles = value_local.reshape(n_uly, TILE, feat_width)

    to_next = from_left[jnp.minimum(slab_now + 1, n_blk - 1)]
    to_prev = from_right[jnp.maximum(slab_now - 1, 0)]
    run_next = (
        lax.dynamic_slice_in_dim(key_tiles, to_next, USED, 0),
        lax.dynamic_slice_in_dim(value_tiles, to_next, USED, 0),
    )
    run_prev = (
        lax.dynamic_slice_in_dim(key_tiles, to_prev, USED, 0),
        lax.dynamic_slice_in_dim(value_tiles, to_prev, USED, 0),
    )
    left_key, left_value = passed_along(run_next, "blk", 1)
    right_key, right_value = passed_along(run_prev, "blk", -1)

    position = jnp.arange(n_uly, dtype=jnp.int32)
    listed = jnp.take(kept_tiles, position * n_blk + slab_now, axis=0)
    is_live = listed >= 0
    safe = jnp.where(is_live, listed, 0)
    relative = safe % n_blk - slab_now
    tile_pos = safe // n_blk
    which = (relative + 1).astype(jnp.int32)
    index = jnp.where(
        relative == 0,
        tile_pos,
        jnp.where(relative < 0, tile_pos - from_left[slab_now], tile_pos - from_right[slab_now]),
    ).astype(jnp.int32)
    index = jnp.where(is_live, index, 0)
    which = jnp.where(is_live, which, 1)
    count = jnp.sum(is_live.astype(jnp.int32), axis=1)

    pieces = []
    for c in range(CHUNKS):
        query_part = lax.all_to_all(
            query_rows[c * chunk:(c + 1) * chunk], "uly", split_axis=1, concat_axis=0, tiled=True
        ).reshape(n_uly, chunk, feat_width)
        attended = attend(
            which.reshape(-1), index.reshape(-1), count,
            query_part, left_key, key_tiles, right_key, left_value, value_tiles, right_value,
        )
        attended = attended.reshape(n_uly * chunk, feat_width)
        pieces.append(lax.all_to_all(attended, "uly", split_axis=0, concat_axis=1, tiled=True))
    return jnp.concatenate(pieces, axis=0)


def solution(mesh):
    placed = (P(("uly", "blk"), None), P(("uly", "blk"), None), P(("uly", "blk"), None), P())
    return jax.shard_map(
        body, mesh=mesh, in_specs=placed, out_specs=P(("uly", "blk"), None), check_vma=False
    )
```

```python
import functools

import jax
import jax.numpy as jnp
from jax import lax
from jax.experimental import pallas as pl
from jax.experimental.pallas import tpu as pltpu
from jax.sharding import PartitionSpec as P

HEAD_DIM = 128
TILE = 384
KEEP = 6
USED = 8
CHUNKS = 1
LOG2_E = 1.4426950408889634


def passed_along(block, axis, distance):
    devices = range(lax.axis_size(axis))
    route = [(i - distance, i) for i in devices if i - distance in devices]
    return lax.ppermute(block, axis, route)


def run_starts(kept_tiles, n_blk, slab_tiles):
    rows = kept_tiles.shape[0]
    row_slab = (jnp.arange(rows, dtype=jnp.int32) % n_blk)[:, None]
    live = kept_tiles >= 0
    entry_slab = jnp.where(live, kept_tiles % n_blk, -5)
    entry_pos = kept_tiles // n_blk
    slabs = jnp.arange(n_blk, dtype=jnp.int32)
    big = jnp.int32(slab_tiles + 1)

    def start_for(shift):
        hit = (row_slab[None] == slabs[:, None, None]) & (
            entry_slab[None] == slabs[:, None, None] + shift
        )
        low = jnp.min(jnp.where(hit, entry_pos[None], big), axis=(1, 2))
        return jnp.where(low == big, 0, jnp.minimum(low, slab_tiles - USED))

    return start_for(-1), start_for(1)


def attend_kernel(which_ref, index_ref, count_ref, q_ref, kl_ref, kc_ref, kr_ref,
                  vl_ref, vc_ref, vr_ref, o_ref):
    i = pl.program_id(0)
    n = count_ref[i]
    score_scale = (HEAD_DIM ** (-0.5)) * LOG2_E
    q = q_ref[0]

    def pick(l_ref, c_ref, r_ref, j):
        w = which_ref[i * KEEP + j]
        x = index_ref[i * KEEP + j]
        side = l_ref.shape[0] - 1
        own = c_ref.shape[0] - 1
        a = l_ref[jnp.clip(x, 0, side)]
        b = c_ref[jnp.clip(x, 0, own)]
        c = r_ref[jnp.clip(x, 0, side)]
        return jnp.where(w == 0, a, jnp.where(w == 1, b, c))

    scores = []
    top = None
    for j in range(KEEP):
        s = jnp.dot(q, pick(kl_ref, kc_ref, kr_ref, j),
                    preferred_element_type=jnp.float32) * score_scale
        if j > 0:
            s = jnp.where(j < n, s, -jnp.inf)
        scores.append(s)
        top = s if top is None else jnp.maximum(top, s)
    m = jnp.max(top, axis=1, keepdims=True)

    spread = None
    acc = None
    for j in range(KEEP):
        p = jnp.exp2(scores[j] - m)
        pv = jnp.dot(p.astype(jnp.bfloat16), pick(vl_ref, vc_ref, vr_ref, j),
                     preferred_element_type=jnp.float32)
        spread = p if spread is None else spread + p
        acc = pv if acc is None else acc + pv
    total = jnp.sum(spread, axis=1, keepdims=True)
    o_ref[0] = (acc / total).astype(o_ref.dtype)


def attend(which, index, count, q, kl, kc, kr, vl, vc, vr):
    n_q, tile, width = q.shape
    key_tile = vc.shape[1]

    def whole(x):
        return pl.BlockSpec(x.shape, lambda i, *_: (0, 0, 0))

    one = pl.BlockSpec((1, tile, width), lambda i, *_: (i, 0, 0))
    grid_spec = pltpu.PrefetchScalarGridSpec(
        num_scalar_prefetch=3,
        grid=(n_q,),
        in_specs=[one] + [whole(x) for x in (kl, kc, kr, vl, vc, vr)],
        out_specs=one,
    )
    cost = pl.CostEstimate(
        flops=n_q * KEEP * tile * key_tile * width * 4,
        transcendentals=n_q * KEEP * tile * key_tile,
        bytes_accessed=2 * (q.size * 2 + (kl.size + kc.size + kr.size) * 2),
    )
    return pl.pallas_call(
        attend_kernel,
        grid_spec=grid_spec,
        out_shape=jax.ShapeDtypeStruct(q.shape, q.dtype),
        compiler_params=pltpu.CompilerParams(dimension_semantics=("arbitrary",)),
        cost_estimate=cost,
    )(which, index, count, q, kl, kc, kr, vl, vc, vr)


def body(query_rows, key_rows, value_rows, kept_tiles):
    key_local, value_local = (
        lax.all_to_all(key_rows, "uly", split_axis=1, concat_axis=0, tiled=True),
        lax.all_to_all(value_rows, "uly", split_axis=1, concat_axis=0, tiled=True),
    )
    n_uly = lax.axis_size("uly")
    n_blk = lax.axis_size("blk")
    feat_width = key_local.shape[1]
    slab_now = lax.axis_index("blk")
    rows = query_rows.shape[0]
    chunk = rows // CHUNKS

    from_left, from_right = run_starts(kept_tiles, n_blk, n_uly)
    key_tiles = jnp.swapaxes(key_local.reshape(n_uly, TILE, feat_width), 1, 2)
    value_tiles = value_local.reshape(n_uly, TILE, feat_width)

    to_next = from_left[jnp.minimum(slab_now + 1, n_blk - 1)]
    to_prev = from_right[jnp.maximum(slab_now - 1, 0)]
    run_next = (
        lax.dynamic_slice_in_dim(key_tiles, to_next, USED, 0),
        lax.dynamic_slice_in_dim(value_tiles, to_next, USED, 0),
    )
    run_prev = (
        lax.dynamic_slice_in_dim(key_tiles, to_prev, USED, 0),
        lax.dynamic_slice_in_dim(value_tiles, to_prev, USED, 0),
    )
    left_key, left_value = passed_along(run_next, "blk", 1)
    right_key, right_value = passed_along(run_prev, "blk", -1)

    position = jnp.arange(n_uly, dtype=jnp.int32)
    listed = jnp.take(kept_tiles, position * n_blk + slab_now, axis=0)
    is_live = listed >= 0
    safe = jnp.where(is_live, listed, 0)
    relative = safe % n_blk - slab_now
    tile_pos = safe // n_blk
    which = (relative + 1).astype(jnp.int32)
    index = jnp.where(
        relative == 0,
        tile_pos,
        jnp.where(relative < 0, tile_pos - from_left[slab_now], tile_pos - from_right[slab_now]),
    ).astype(jnp.int32)
    index = jnp.where(is_live, index, 0)
    which = jnp.where(is_live, which, 1)
    count = jnp.sum(is_live.astype(jnp.int32), axis=1)

    pieces = []
    for c in range(CHUNKS):
        query_part = lax.all_to_all(
            query_rows[c * chunk:(c + 1) * chunk], "uly", split_axis=1, concat_axis=0, tiled=True
        ).reshape(n_uly, chunk, feat_width)
        attended = attend(
            which.reshape(-1), index.reshape(-1), count,
            query_part, left_key, key_tiles, right_key, left_value, value_tiles, right_value,
        )
        attended = attended.reshape(n_uly * chunk, feat_width)
        pieces.append(lax.all_to_all(attended, "uly", split_axis=0, concat_axis=1, tiled=True))
    return jnp.concatenate(pieces, axis=0)


def solution(mesh):
    placed = (P(("uly", "blk"), None), P(("uly", "blk"), None), P(("uly", "blk"), None), P())
    return jax.shard_map(
        body, mesh=mesh, in_specs=placed, out_specs=P(("uly", "blk"), None), check_vma=False
    )
```

```python
import functools

import jax
import jax.numpy as jnp
from jax import lax
from jax.experimental import pallas as pl
from jax.experimental.pallas import tpu as pltpu
from jax.sharding import PartitionSpec as P

HEAD_DIM = 128
TILE = 384
KEEP = 6
USED = 8
CHUNKS = 1
LOG2_E = 1.4426950408889634


def passed_along(block, axis, distance):
    devices = range(lax.axis_size(axis))
    route = [(i - distance, i) for i in devices if i - distance in devices]
    return lax.ppermute(block, axis, route)


def run_starts(kept_tiles, n_blk, slab_tiles):
    rows = kept_tiles.shape[0]
    row_slab = (jnp.arange(rows, dtype=jnp.int32) % n_blk)[:, None]
    live = kept_tiles >= 0
    entry_slab = jnp.where(live, kept_tiles % n_blk, -5)
    entry_pos = kept_tiles // n_blk
    slabs = jnp.arange(n_blk, dtype=jnp.int32)
    big = jnp.int32(slab_tiles + 1)

    def start_for(shift):
        hit = (row_slab[None] == slabs[:, None, None]) & (
            entry_slab[None] == slabs[:, None, None] + shift
        )
        low = jnp.min(jnp.where(hit, entry_pos[None], big), axis=(1, 2))
        return jnp.where(low == big, 0, jnp.minimum(low, slab_tiles - USED))

    return start_for(-1), start_for(1)


def attend_kernel(which_ref, index_ref, count_ref, q_ref, kl_ref, kc_ref, kr_ref,
                  vl_ref, vc_ref, vr_ref, o_ref):
    i = pl.program_id(0)
    n = count_ref[i]
    score_scale = (HEAD_DIM ** (-0.5)) * LOG2_E
    q = q_ref[0]

    def pick(l_ref, c_ref, r_ref, j):
        w = which_ref[i * KEEP + j]
        x = index_ref[i * KEEP + j]
        side = l_ref.shape[0] - 1
        own = c_ref.shape[0] - 1
        a = l_ref[jnp.clip(x, 0, side)]
        b = c_ref[jnp.clip(x, 0, own)]
        c = r_ref[jnp.clip(x, 0, side)]
        return jnp.where(w == 0, a, jnp.where(w == 1, b, c))

    scores = []
    top = None
    for j in range(KEEP):
        s = jnp.dot(q, pick(kl_ref, kc_ref, kr_ref, j),
                    preferred_element_type=jnp.float32) * score_scale
        if j > 0:
            s = jnp.where(j < n, s, -jnp.inf)
        scores.append(s)
        top = s if top is None else jnp.maximum(top, s)
    m = jnp.max(top, axis=1, keepdims=True)

    spread = None
    acc = None
    for j in range(KEEP):
        p = jnp.exp2(scores[j] - m)
        pv = jnp.dot(p.astype(jnp.bfloat16), pick(vl_ref, vc_ref, vr_ref, j),
                     preferred_element_type=jnp.float32)
        spread = p if spread is None else spread + p
        acc = pv if acc is None else acc + pv
    total = jnp.sum(spread, axis=1, keepdims=True)
    o_ref[0] = (acc / total).astype(o_ref.dtype)


def attend(which, index, count, q, kl, kc, kr, vl, vc, vr):
    n_q, tile, width = q.shape
    key_tile = vc.shape[1]

    def whole(x):
        return pl.BlockSpec(x.shape, lambda i, *_: (0, 0, 0))

    one = pl.BlockSpec((1, tile, width), lambda i, *_: (i, 0, 0))
    grid_spec = pltpu.PrefetchScalarGridSpec(
        num_scalar_prefetch=3,
        grid=(n_q,),
        in_specs=[one] + [whole(x) for x in (kl, kc, kr, vl, vc, vr)],
        out_specs=one,
    )
    cost = pl.CostEstimate(
        flops=n_q * KEEP * tile * key_tile * width * 4,
        transcendentals=n_q * KEEP * tile * key_tile,
        bytes_accessed=2 * (q.size * 2 + (kl.size + kc.size + kr.size) * 2),
    )
    return pl.pallas_call(
        attend_kernel,
        grid_spec=grid_spec,
        out_shape=jax.ShapeDtypeStruct(q.shape, q.dtype),
        compiler_params=pltpu.CompilerParams(dimension_semantics=("arbitrary",)),
        cost_estimate=cost,
    )(which, index, count, q, kl, kc, kr, vl, vc, vr)


def body(query_rows, key_rows, value_rows, kept_tiles):
    n_uly = lax.axis_size("uly")
    n_blk = lax.axis_size("blk")
    rows, width = query_rows.shape
    feat_width = width // n_uly
    stacked = jnp.stack(
        [x.reshape(rows, n_uly, feat_width) for x in (query_rows, key_rows, value_rows)]
    )
    stacked = lax.all_to_all(stacked, "uly", split_axis=2, concat_axis=1, tiled=True)
    query_local, key_local, value_local = (
        stacked[0].reshape(n_uly * rows, feat_width),
        stacked[1].reshape(n_uly * rows, feat_width),
        stacked[2].reshape(n_uly * rows, feat_width),
    )
    slab_now = lax.axis_index("blk")
    chunk = rows // CHUNKS

    from_left, from_right = run_starts(kept_tiles, n_blk, n_uly)
    key_tiles = jnp.swapaxes(key_local.reshape(n_uly, TILE, feat_width), 1, 2)
    value_tiles = value_local.reshape(n_uly, TILE, feat_width)

    to_next = from_left[jnp.minimum(slab_now + 1, n_blk - 1)]
    to_prev = from_right[jnp.maximum(slab_now - 1, 0)]
    run_next = (
        lax.dynamic_slice_in_dim(key_tiles, to_next, USED, 0),
        lax.dynamic_slice_in_dim(value_tiles, to_next, USED, 0),
    )
    run_prev = (
        lax.dynamic_slice_in_dim(key_tiles, to_prev, USED, 0),
        lax.dynamic_slice_in_dim(value_tiles, to_prev, USED, 0),
    )
    left_key, left_value = passed_along(run_next, "blk", 1)
    right_key, right_value = passed_along(run_prev, "blk", -1)

    position = jnp.arange(n_uly, dtype=jnp.int32)
    listed = jnp.take(kept_tiles, position * n_blk + slab_now, axis=0)
    is_live = listed >= 0
    safe = jnp.where(is_live, listed, 0)
    relative = safe % n_blk - slab_now
    tile_pos = safe // n_blk
    which = (relative + 1).astype(jnp.int32)
    index = jnp.where(
        relative == 0,
        tile_pos,
        jnp.where(relative < 0, tile_pos - from_left[slab_now], tile_pos - from_right[slab_now]),
    ).astype(jnp.int32)
    index = jnp.where(is_live, index, 0)
    which = jnp.where(is_live, which, 1)
    count = jnp.sum(is_live.astype(jnp.int32), axis=1)

    query_tiles = query_local.reshape(n_uly, rows, feat_width)
    pieces = []
    for c in range(CHUNKS):
        query_part = query_tiles[:, c * chunk:(c + 1) * chunk]
        attended = attend(
            which.reshape(-1), index.reshape(-1), count,
            query_part, left_key, key_tiles, right_key, left_value, value_tiles, right_value,
        )
        attended = attended.reshape(n_uly * chunk, feat_width)
        pieces.append(lax.all_to_all(attended, "uly", split_axis=0, concat_axis=1, tiled=True))
    return jnp.concatenate(pieces, axis=0)


def solution(mesh):
    placed = (P(("uly", "blk"), None), P(("uly", "blk"), None), P(("uly", "blk"), None), P())
    return jax.shard_map(
        body, mesh=mesh, in_specs=placed, out_specs=P(("uly", "blk"), None), check_vma=False
    )
```

```python
import functools

import jax
import jax.numpy as jnp
from jax import lax
from jax.experimental import pallas as pl
from jax.experimental.pallas import tpu as pltpu
from jax.sharding import PartitionSpec as P

HEAD_DIM = 128
TILE = 384
KEEP = 6
USED = 8
CHUNKS = 1
GROUP = 4
LOG2_E = 1.4426950408889634


def passed_along(block, axis, distance):
    devices = range(lax.axis_size(axis))
    route = [(i - distance, i) for i in devices if i - distance in devices]
    return lax.ppermute(block, axis, route)


def run_starts(kept_tiles, n_blk, slab_tiles):
    rows = kept_tiles.shape[0]
    row_slab = (jnp.arange(rows, dtype=jnp.int32) % n_blk)[:, None]
    live = kept_tiles >= 0
    entry_slab = jnp.where(live, kept_tiles % n_blk, -5)
    entry_pos = kept_tiles // n_blk
    slabs = jnp.arange(n_blk, dtype=jnp.int32)
    big = jnp.int32(slab_tiles + 1)

    def start_for(shift):
        hit = (row_slab[None] == slabs[:, None, None]) & (
            entry_slab[None] == slabs[:, None, None] + shift
        )
        low = jnp.min(jnp.where(hit, entry_pos[None], big), axis=(1, 2))
        return jnp.where(low == big, 0, jnp.minimum(low, slab_tiles - USED))

    return start_for(-1), start_for(1)


def attend_kernel(which_ref, index_ref, count_ref, q_ref, kl_ref, kc_ref, kr_ref,
                  vl_ref, vc_ref, vr_ref, o_ref):
    for g in range(q_ref.shape[0]):
        attend_one(g, pl.program_id(0) * q_ref.shape[0] + g, which_ref, index_ref, count_ref,
                   q_ref, kl_ref, kc_ref, kr_ref, vl_ref, vc_ref, vr_ref, o_ref)


def attend_one(g, i, which_ref, index_ref, count_ref, q_ref, kl_ref, kc_ref, kr_ref,
               vl_ref, vc_ref, vr_ref, o_ref):
    n = count_ref[i]
    score_scale = (HEAD_DIM ** (-0.5)) * LOG2_E
    q = q_ref[g]

    def pick(l_ref, c_ref, r_ref, j):
        w = which_ref[i * KEEP + j]
        x = index_ref[i * KEEP + j]
        side = l_ref.shape[0] - 1
        own = c_ref.shape[0] - 1
        a = l_ref[jnp.clip(x, 0, side)]
        b = c_ref[jnp.clip(x, 0, own)]
        c = r_ref[jnp.clip(x, 0, side)]
        return jnp.where(w == 0, a, jnp.where(w == 1, b, c))

    scores = []
    top = None
    for j in range(KEEP):
        s = jnp.dot(q, pick(kl_ref, kc_ref, kr_ref, j),
                    preferred_element_type=jnp.float32) * score_scale
        if j > 0:
            s = jnp.where(j < n, s, -jnp.inf)
        scores.append(s)
        top = s if top is None else jnp.maximum(top, s)
    m = jnp.max(top, axis=1, keepdims=True)

    spread = None
    acc = None
    for j in range(KEEP):
        p = jnp.exp2(scores[j] - m)
        pv = jnp.dot(p.astype(jnp.bfloat16), pick(vl_ref, vc_ref, vr_ref, j),
                     preferred_element_type=jnp.float32)
        spread = p if spread is None else spread + p
        acc = pv if acc is None else acc + pv
    total = jnp.sum(spread, axis=1, keepdims=True)
    o_ref[g] = (acc / total).astype(o_ref.dtype)


def attend(which, index, count, q, kl, kc, kr, vl, vc, vr):
    n_q, tile, width = q.shape
    key_tile = vc.shape[1]

    def whole(x):
        return pl.BlockSpec(x.shape, lambda i, *_: (0, 0, 0))

    group = GROUP if n_q % GROUP == 0 else 1
    one = pl.BlockSpec((group, tile, width), lambda i, *_: (i, 0, 0))
    grid_spec = pltpu.PrefetchScalarGridSpec(
        num_scalar_prefetch=3,
        grid=(n_q // group,),
        in_specs=[one] + [whole(x) for x in (kl, kc, kr, vl, vc, vr)],
        out_specs=one,
    )
    cost = pl.CostEstimate(
        flops=n_q * KEEP * tile * key_tile * width * 4,
        transcendentals=n_q * KEEP * tile * key_tile,
        bytes_accessed=2 * (q.size * 2 + (kl.size + kc.size + kr.size) * 2),
    )
    return pl.pallas_call(
        attend_kernel,
        grid_spec=grid_spec,
        out_shape=jax.ShapeDtypeStruct(q.shape, q.dtype),
        compiler_params=pltpu.CompilerParams(dimension_semantics=("arbitrary",)),
        cost_estimate=cost,
    )(which, index, count, q, kl, kc, kr, vl, vc, vr)


def body(query_rows, key_rows, value_rows, kept_tiles):
    key_local, value_local = (
        lax.all_to_all(key_rows, "uly", split_axis=1, concat_axis=0, tiled=True),
        lax.all_to_all(value_rows, "uly", split_axis=1, concat_axis=0, tiled=True),
    )
    n_uly = lax.axis_size("uly")
    n_blk = lax.axis_size("blk")
    feat_width = key_local.shape[1]
    slab_now = lax.axis_index("blk")
    rows = query_rows.shape[0]
    chunk = rows // CHUNKS

    from_left, from_right = run_starts(kept_tiles, n_blk, n_uly)
    key_tiles = jnp.swapaxes(key_local.reshape(n_uly, TILE, feat_width), 1, 2)
    value_tiles = value_local.reshape(n_uly, TILE, feat_width)

    to_next = from_left[jnp.minimum(slab_now + 1, n_blk - 1)]
    to_prev = from_right[jnp.maximum(slab_now - 1, 0)]
    run_next = (
        lax.dynamic_slice_in_dim(key_tiles, to_next, USED, 0),
        lax.dynamic_slice_in_dim(value_tiles, to_next, USED, 0),
    )
    run_prev = (
        lax.dynamic_slice_in_dim(key_tiles, to_prev, USED, 0),
        lax.dynamic_slice_in_dim(value_tiles, to_prev, USED, 0),
    )
    left_key, left_value = passed_along(run_next, "blk", 1)
    right_key, right_value = passed_along(run_prev, "blk", -1)

    position = jnp.arange(n_uly, dtype=jnp.int32)
    listed = jnp.take(kept_tiles, position * n_blk + slab_now, axis=0)
    is_live = listed >= 0
    safe = jnp.where(is_live, listed, 0)
    relative = safe % n_blk - slab_now
    tile_pos = safe // n_blk
    which = (relative + 1).astype(jnp.int32)
    index = jnp.where(
        relative == 0,
        tile_pos,
        jnp.where(relative < 0, tile_pos - from_left[slab_now], tile_pos - from_right[slab_now]),
    ).astype(jnp.int32)
    index = jnp.where(is_live, index, 0)
    which = jnp.where(is_live, which, 1)
    count = jnp.sum(is_live.astype(jnp.int32), axis=1)

    pieces = []
    for c in range(CHUNKS):
        query_part = lax.all_to_all(
            query_rows[c * chunk:(c + 1) * chunk], "uly", split_axis=1, concat_axis=0, tiled=True
        ).reshape(n_uly, chunk, feat_width)
        attended = attend(
            which.reshape(-1), index.reshape(-1), count,
            query_part, left_key, key_tiles, right_key, left_value, value_tiles, right_value,
        )
        attended = attended.reshape(n_uly * chunk, feat_width)
        pieces.append(lax.all_to_all(attended, "uly", split_axis=0, concat_axis=1, tiled=True))
    return jnp.concatenate(pieces, axis=0)


def solution(mesh):
    placed = (P(("uly", "blk"), None), P(("uly", "blk"), None), P(("uly", "blk"), None), P())
    return jax.shard_map(
        body, mesh=mesh, in_specs=placed, out_specs=P(("uly", "blk"), None), check_vma=False
    )
```

```python
import functools

import jax
import jax.numpy as jnp
from jax import lax
from jax.experimental import pallas as pl
from jax.experimental.pallas import tpu as pltpu
from jax.sharding import PartitionSpec as P

HEAD_DIM = 128
TILE = 384
KEEP = 6
USED = 8
CHUNKS = 1
GROUP = 4
LOG2_E = 1.4426950408889634


def passed_along(block, axis, distance):
    devices = range(lax.axis_size(axis))
    route = [(i - distance, i) for i in devices if i - distance in devices]
    return lax.ppermute(block, axis, route)


def run_starts(kept_tiles, n_blk, slab_tiles):
    rows = kept_tiles.shape[0]
    row_slab = (jnp.arange(rows, dtype=jnp.int32) % n_blk)[:, None]
    live = kept_tiles >= 0
    entry_slab = jnp.where(live, kept_tiles % n_blk, -5)
    entry_pos = kept_tiles // n_blk
    slabs = jnp.arange(n_blk, dtype=jnp.int32)
    big = jnp.int32(slab_tiles + 1)

    def start_for(shift):
        hit = (row_slab[None] == slabs[:, None, None]) & (
            entry_slab[None] == slabs[:, None, None] + shift
        )
        low = jnp.min(jnp.where(hit, entry_pos[None], big), axis=(1, 2))
        return jnp.where(low == big, 0, jnp.minimum(low, slab_tiles - USED))

    return start_for(-1), start_for(1)


def attend_kernel(which_ref, index_ref, count_ref, q_ref, kl_ref, kc_ref, kr_ref,
                  vl_ref, vc_ref, vr_ref, o_ref):
    for g in range(q_ref.shape[0]):
        attend_one(g, pl.program_id(0) * q_ref.shape[0] + g, which_ref, index_ref, count_ref,
                   q_ref, kl_ref, kc_ref, kr_ref, vl_ref, vc_ref, vr_ref, o_ref)


def attend_one(g, i, which_ref, index_ref, count_ref, q_ref, kl_ref, kc_ref, kr_ref,
               vl_ref, vc_ref, vr_ref, o_ref):
    n = count_ref[i]
    score_scale = (HEAD_DIM ** (-0.5)) * LOG2_E
    q = q_ref[g]

    def pick(l_ref, c_ref, r_ref, j):
        w = which_ref[i * KEEP + j]
        x = index_ref[i * KEEP + j]
        side = l_ref.shape[0] - 1
        own = c_ref.shape[0] - 1
        a = l_ref[jnp.clip(x, 0, side)]
        b = c_ref[jnp.clip(x, 0, own)]
        c = r_ref[jnp.clip(x, 0, side)]
        return jnp.where(w == 0, a, jnp.where(w == 1, b, c))

    scores = []
    top = None
    for j in range(KEEP):
        s = jnp.dot(q, pick(kl_ref, kc_ref, kr_ref, j),
                    preferred_element_type=jnp.float32) * score_scale
        if j > 0:
            s = jnp.where(j < n, s, -jnp.inf)
        scores.append(s)
        top = s if top is None else jnp.maximum(top, s)
    m = jnp.max(top, axis=1, keepdims=True)

    spread = None
    acc = None
    for j in range(KEEP):
        p = jnp.exp2(scores[j] - m)
        pv = jnp.dot(p.astype(jnp.bfloat16), pick(vl_ref, vc_ref, vr_ref, j),
                     preferred_element_type=jnp.float32)
        spread = p if spread is None else spread + p
        acc = pv if acc is None else acc + pv
    total = jnp.sum(spread, axis=1, keepdims=True)
    o_ref[g] = (acc / total).astype(o_ref.dtype)


def attend(which, index, count, q, kl, kc, kr, vl, vc, vr):
    n_q, tile, width = q.shape
    key_tile = vc.shape[1]

    def whole(x):
        return pl.BlockSpec(x.shape, lambda i, *_: (0, 0, 0))

    group = GROUP if n_q % GROUP == 0 else 1
    one = pl.BlockSpec((group, tile, width), lambda i, *_: (i, 0, 0))
    grid_spec = pltpu.PrefetchScalarGridSpec(
        num_scalar_prefetch=3,
        grid=(n_q // group,),
        in_specs=[one] + [whole(x) for x in (kl, kc, kr, vl, vc, vr)],
        out_specs=one,
    )
    cost = pl.CostEstimate(
        flops=n_q * KEEP * tile * key_tile * width * 4,
        transcendentals=n_q * KEEP * tile * key_tile,
        bytes_accessed=2 * (q.size * 2 + (kl.size + kc.size + kr.size) * 2),
    )
    return pl.pallas_call(
        attend_kernel,
        grid_spec=grid_spec,
        out_shape=jax.ShapeDtypeStruct(q.shape, q.dtype),
        compiler_params=pltpu.CompilerParams(dimension_semantics=("arbitrary",)),
        cost_estimate=cost,
    )(which, index, count, q, kl, kc, kr, vl, vc, vr)


def spread_query(query_rows, n_uly, feat_width):
    rows = query_rows.shape[0]
    side = int(round(n_uly ** 0.5))
    if side * side != n_uly:
        side = 1
    width = n_uly // side
    heads = jnp.transpose(query_rows.reshape(rows, n_uly, feat_width), (1, 0, 2))
    me = lax.axis_index("uly")
    my_y, my_x = me // width, me % width
    received = [lax.dynamic_index_in_dim(heads, me, 0, keepdims=False)]
    for shift in range(1, n_uly):
        dy, dx = divmod(shift, width)
        pairs = [(v, ((v // width + dy) % side) * width + (v % width + dx) % width)
                 for v in range(n_uly)]
        target = ((my_y + dy) % side) * width + (my_x + dx) % width
        block = lax.dynamic_index_in_dim(heads, target, 0, keepdims=False)
        received.append(lax.ppermute(block, "uly", pairs))
    stacked = jnp.stack(received)
    position = jnp.arange(n_uly, dtype=jnp.int32)
    came_by = ((my_y - position // width) % side) * width + (my_x - position % width) % width
    return jnp.take(stacked, came_by, axis=0)


def body(query_rows, key_rows, value_rows, kept_tiles):
    key_local, value_local = (
        lax.all_to_all(key_rows, "uly", split_axis=1, concat_axis=0, tiled=True),
        lax.all_to_all(value_rows, "uly", split_axis=1, concat_axis=0, tiled=True),
    )
    n_uly = lax.axis_size("uly")
    n_blk = lax.axis_size("blk")
    feat_width = key_local.shape[1]
    slab_now = lax.axis_index("blk")
    rows = query_rows.shape[0]
    chunk = rows // CHUNKS

    from_left, from_right = run_starts(kept_tiles, n_blk, n_uly)
    key_tiles = jnp.swapaxes(key_local.reshape(n_uly, TILE, feat_width), 1, 2)
    value_tiles = value_local.reshape(n_uly, TILE, feat_width)

    to_next = from_left[jnp.minimum(slab_now + 1, n_blk - 1)]
    to_prev = from_right[jnp.maximum(slab_now - 1, 0)]
    run_next = (
        lax.dynamic_slice_in_dim(key_tiles, to_next, USED, 0),
        lax.dynamic_slice_in_dim(value_tiles, to_next, USED, 0),
    )
    run_prev = (
        lax.dynamic_slice_in_dim(key_tiles, to_prev, USED, 0),
        lax.dynamic_slice_in_dim(value_tiles, to_prev, USED, 0),
    )
    left_key, left_value = passed_along(run_next, "blk", 1)
    right_key, right_value = passed_along(run_prev, "blk", -1)

    position = jnp.arange(n_uly, dtype=jnp.int32)
    listed = jnp.take(kept_tiles, position * n_blk + slab_now, axis=0)
    is_live = listed >= 0
    safe = jnp.where(is_live, listed, 0)
    relative = safe % n_blk - slab_now
    tile_pos = safe // n_blk
    which = (relative + 1).astype(jnp.int32)
    index = jnp.where(
        relative == 0,
        tile_pos,
        jnp.where(relative < 0, tile_pos - from_left[slab_now], tile_pos - from_right[slab_now]),
    ).astype(jnp.int32)
    index = jnp.where(is_live, index, 0)
    which = jnp.where(is_live, which, 1)
    count = jnp.sum(is_live.astype(jnp.int32), axis=1)

    pieces = []
    for c in range(CHUNKS):
        query_part = spread_query(query_rows[c * chunk:(c + 1) * chunk], n_uly, feat_width)
        attended = attend(
            which.reshape(-1), index.reshape(-1), count,
            query_part, left_key, key_tiles, right_key, left_value, value_tiles, right_value,
        )
        attended = attended.reshape(n_uly * chunk, feat_width)
        pieces.append(lax.all_to_all(attended, "uly", split_axis=0, concat_axis=1, tiled=True))
    return jnp.concatenate(pieces, axis=0)


def solution(mesh):
    placed = (P(("uly", "blk"), None), P(("uly", "blk"), None), P(("uly", "blk"), None), P())
    return jax.shard_map(
        body, mesh=mesh, in_specs=placed, out_specs=P(("uly", "blk"), None), check_vma=False
    )
```

```python
import functools

import jax
import jax.numpy as jnp
from jax import lax
from jax.experimental import pallas as pl
from jax.experimental.pallas import tpu as pltpu
from jax.sharding import PartitionSpec as P

HEAD_DIM = 128
TILE = 384
KEEP = 6
USED = 8
CHUNKS = 1
GROUP = 4
LOG2_E = 1.4426950408889634


def passed_along(block, axis, distance):
    devices = range(lax.axis_size(axis))
    route = [(i - distance, i) for i in devices if i - distance in devices]
    return lax.ppermute(block, axis, route)


def run_starts(kept_tiles, n_blk, slab_tiles):
    rows = kept_tiles.shape[0]
    row_slab = (jnp.arange(rows, dtype=jnp.int32) % n_blk)[:, None]
    live = kept_tiles >= 0
    entry_slab = jnp.where(live, kept_tiles % n_blk, -5)
    entry_pos = kept_tiles // n_blk
    slabs = jnp.arange(n_blk, dtype=jnp.int32)
    big = jnp.int32(slab_tiles + 1)

    def start_for(shift):
        hit = (row_slab[None] == slabs[:, None, None]) & (
            entry_slab[None] == slabs[:, None, None] + shift
        )
        low = jnp.min(jnp.where(hit, entry_pos[None], big), axis=(1, 2))
        return jnp.where(low == big, 0, jnp.minimum(low, slab_tiles - USED))

    return start_for(-1), start_for(1)


def attend_kernel(which_ref, index_ref, count_ref, q_ref, kl_ref, kc_ref, kr_ref,
                  vl_hbm, vc_hbm, vr_hbm, o_ref, vl_ref, vc_ref, vr_ref, sems):
    first = pl.program_id(0) == 0
    loads = [pltpu.make_async_copy(src, dst, sems.at[k])
             for k, (src, dst) in enumerate(((vl_hbm, vl_ref), (vc_hbm, vc_ref), (vr_hbm, vr_ref)))]

    @pl.when(first)
    def _():
        for load in loads:
            load.start()

    def values_ready():
        @pl.when(first)
        def _():
            for load in loads:
                load.wait()

    for g in range(q_ref.shape[0]):
        attend_one(g, pl.program_id(0) * q_ref.shape[0] + g, which_ref, index_ref, count_ref,
                   q_ref, kl_ref, kc_ref, kr_ref, vl_ref, vc_ref, vr_ref, o_ref,
                   values_ready if g == 0 else None)


def attend_one(g, i, which_ref, index_ref, count_ref, q_ref, kl_ref, kc_ref, kr_ref,
               vl_ref, vc_ref, vr_ref, o_ref, before_values=None):
    n = count_ref[i]
    score_scale = (HEAD_DIM ** (-0.5)) * LOG2_E
    q = q_ref[g]

    def pick(l_ref, c_ref, r_ref, j):
        w = which_ref[i * KEEP + j]
        x = index_ref[i * KEEP + j]
        side = l_ref.shape[0] - 1
        own = c_ref.shape[0] - 1
        a = l_ref[jnp.clip(x, 0, side)]
        b = c_ref[jnp.clip(x, 0, own)]
        c = r_ref[jnp.clip(x, 0, side)]
        return jnp.where(w == 0, a, jnp.where(w == 1, b, c))

    scores = []
    top = None
    for j in range(KEEP):
        s = jnp.dot(q, pick(kl_ref, kc_ref, kr_ref, j),
                    preferred_element_type=jnp.float32) * score_scale
        if j > 0:
            s = jnp.where(j < n, s, -jnp.inf)
        scores.append(s)
        top = s if top is None else jnp.maximum(top, s)
    m = jnp.max(top, axis=1, keepdims=True)
    if before_values is not None:
        before_values()

    spread = None
    acc = None
    for j in range(KEEP):
        p = jnp.exp2(scores[j] - m)
        pv = jnp.dot(p.astype(jnp.bfloat16), pick(vl_ref, vc_ref, vr_ref, j),
                     preferred_element_type=jnp.float32)
        spread = p if spread is None else spread + p
        acc = pv if acc is None else acc + pv
    total = jnp.sum(spread, axis=1, keepdims=True)
    o_ref[g] = (acc / total).astype(o_ref.dtype)


def attend(which, index, count, q, kl, kc, kr, vl, vc, vr):
    n_q, tile, width = q.shape
    key_tile = vc.shape[1]

    def whole(x):
        return pl.BlockSpec(x.shape, lambda i, *_: (0, 0, 0))

    group = GROUP if n_q % GROUP == 0 else 1
    one = pl.BlockSpec((group, tile, width), lambda i, *_: (i, 0, 0))
    grid_spec = pltpu.PrefetchScalarGridSpec(
        num_scalar_prefetch=3,
        grid=(n_q // group,),
        in_specs=[one] + [whole(x) for x in (kl, kc, kr)]
        + [pl.BlockSpec(memory_space=pl.ANY)] * 3,
        out_specs=one,
        scratch_shapes=[pltpu.VMEM(x.shape, x.dtype) for x in (vl, vc, vr)]
        + [pltpu.SemaphoreType.DMA((3,))],
    )
    cost = pl.CostEstimate(
        flops=n_q * KEEP * tile * key_tile * width * 4,
        transcendentals=n_q * KEEP * tile * key_tile,
        bytes_accessed=2 * (q.size * 2 + (kl.size + kc.size + kr.size) * 2),
    )
    return pl.pallas_call(
        attend_kernel,
        grid_spec=grid_spec,
        out_shape=jax.ShapeDtypeStruct(q.shape, q.dtype),
        compiler_params=pltpu.CompilerParams(dimension_semantics=("arbitrary",)),
        cost_estimate=cost,
    )(which, index, count, q, kl, kc, kr, vl, vc, vr)


def body(query_rows, key_rows, value_rows, kept_tiles):
    key_local, value_local = (
        lax.all_to_all(key_rows, "uly", split_axis=1, concat_axis=0, tiled=True),
        lax.all_to_all(value_rows, "uly", split_axis=1, concat_axis=0, tiled=True),
    )
    n_uly = lax.axis_size("uly")
    n_blk = lax.axis_size("blk")
    feat_width = key_local.shape[1]
    slab_now = lax.axis_index("blk")
    rows = query_rows.shape[0]
    chunk = rows // CHUNKS

    from_left, from_right = run_starts(kept_tiles, n_blk, n_uly)
    key_tiles = jnp.swapaxes(key_local.reshape(n_uly, TILE, feat_width), 1, 2)
    value_tiles = value_local.reshape(n_uly, TILE, feat_width)

    to_next = from_left[jnp.minimum(slab_now + 1, n_blk - 1)]
    to_prev = from_right[jnp.maximum(slab_now - 1, 0)]
    run_next = (
        lax.dynamic_slice_in_dim(key_tiles, to_next, USED, 0),
        lax.dynamic_slice_in_dim(value_tiles, to_next, USED, 0),
    )
    run_prev = (
        lax.dynamic_slice_in_dim(key_tiles, to_prev, USED, 0),
        lax.dynamic_slice_in_dim(value_tiles, to_prev, USED, 0),
    )
    left_key, left_value = passed_along(run_next, "blk", 1)
    right_key, right_value = passed_along(run_prev, "blk", -1)

    position = jnp.arange(n_uly, dtype=jnp.int32)
    listed = jnp.take(kept_tiles, position * n_blk + slab_now, axis=0)
    is_live = listed >= 0
    safe = jnp.where(is_live, listed, 0)
    relative = safe % n_blk - slab_now
    tile_pos = safe // n_blk
    which = (relative + 1).astype(jnp.int32)
    index = jnp.where(
        relative == 0,
        tile_pos,
        jnp.where(relative < 0, tile_pos - from_left[slab_now], tile_pos - from_right[slab_now]),
    ).astype(jnp.int32)
    index = jnp.where(is_live, index, 0)
    which = jnp.where(is_live, which, 1)
    count = jnp.sum(is_live.astype(jnp.int32), axis=1)

    pieces = []
    for c in range(CHUNKS):
        query_part = lax.all_to_all(
            query_rows[c * chunk:(c + 1) * chunk], "uly", split_axis=1, concat_axis=0, tiled=True
        ).reshape(n_uly, chunk, feat_width)
        attended = attend(
            which.reshape(-1), index.reshape(-1), count,
            query_part, left_key, key_tiles, right_key, left_value, value_tiles, right_value,
        )
        attended = attended.reshape(n_uly * chunk, feat_width)
        pieces.append(lax.all_to_all(attended, "uly", split_axis=0, concat_axis=1, tiled=True))
    return jnp.concatenate(pieces, axis=0)


def solution(mesh):
    placed = (P(("uly", "blk"), None), P(("uly", "blk"), None), P(("uly", "blk"), None), P())
    return jax.shard_map(
        body, mesh=mesh, in_specs=placed, out_specs=P(("uly", "blk"), None), check_vma=False
    )
```

```python
import functools

import jax
import jax.numpy as jnp
from jax import lax
from jax.experimental import pallas as pl
from jax.experimental.pallas import tpu as pltpu
from jax.sharding import PartitionSpec as P

HEAD_DIM = 128
TILE = 384
KEEP = 6
USED = 8
CHUNKS = 1
GROUP = 4
LOG2_E = 1.4426950408889634


def passed_along(block, axis, distance):
    devices = range(lax.axis_size(axis))
    route = [(i - distance, i) for i in devices if i - distance in devices]
    return lax.ppermute(block, axis, route)


def run_starts(kept_tiles, n_blk, slab_tiles):
    rows = kept_tiles.shape[0]
    row_slab = (jnp.arange(rows, dtype=jnp.int32) % n_blk)[:, None]
    live = kept_tiles >= 0
    entry_slab = jnp.where(live, kept_tiles % n_blk, -5)
    entry_pos = kept_tiles // n_blk
    slabs = jnp.arange(n_blk, dtype=jnp.int32)
    big = jnp.int32(slab_tiles + 1)

    def start_for(shift):
        hit = (row_slab[None] == slabs[:, None, None]) & (
            entry_slab[None] == slabs[:, None, None] + shift
        )
        low = jnp.min(jnp.where(hit, entry_pos[None], big), axis=(1, 2))
        return jnp.where(low == big, 0, jnp.minimum(low, slab_tiles - USED))

    return start_for(-1), start_for(1)


def attend_kernel(which_ref, index_ref, count_ref, q_ref, kl_ref, kc_ref, kr_ref,
                  vl_ref, vc_ref, vr_ref, o_ref):
    for g in range(q_ref.shape[0]):
        attend_one(g, pl.program_id(0) * q_ref.shape[0] + g, which_ref, index_ref, count_ref,
                   q_ref, kl_ref, kc_ref, kr_ref, vl_ref, vc_ref, vr_ref, o_ref)


def attend_one(g, i, which_ref, index_ref, count_ref, q_ref, kl_ref, kc_ref, kr_ref,
               vl_ref, vc_ref, vr_ref, o_ref):
    n = count_ref[i]
    score_scale = (HEAD_DIM ** (-0.5)) * LOG2_E
    q = q_ref[g]

    def pick(l_ref, c_ref, r_ref, j):
        w = which_ref[i * KEEP + j]
        x = index_ref[i * KEEP + j]
        side = l_ref.shape[0] - 1
        own = c_ref.shape[0] - 1
        a = l_ref[jnp.clip(x, 0, side)]
        b = c_ref[jnp.clip(x, 0, own)]
        c = r_ref[jnp.clip(x, 0, side)]
        return jnp.where(w == 0, a, jnp.where(w == 1, b, c))

    scores = []
    top = None
    for j in range(KEEP):
        s = jnp.dot(q, pick(kl_ref, kc_ref, kr_ref, j),
                    preferred_element_type=jnp.float32) * score_scale
        if j > 0:
            s = jnp.where(j < n, s, -jnp.inf)
        scores.append(s)
        top = s if top is None else jnp.maximum(top, s)
    m = jnp.max(top, axis=1, keepdims=True)

    spread = None
    acc = None
    for j in range(KEEP):
        p = jnp.exp2(scores[j] - m)
        pv = jnp.dot(p.astype(jnp.bfloat16), pick(vl_ref, vc_ref, vr_ref, j),
                     preferred_element_type=jnp.float32)
        spread = p if spread is None else spread + p
        acc = pv if acc is None else acc + pv
    total = jnp.sum(spread, axis=1, keepdims=True)
    o_ref[g] = (acc / total).astype(o_ref.dtype)


def attend(which, index, count, q, kl, kc, kr, vl, vc, vr):
    n_q, tile, width = q.shape
    key_tile = vc.shape[1]

    def whole(x):
        return pl.BlockSpec(x.shape, lambda i, *_: (0, 0, 0))

    group = GROUP if n_q % GROUP == 0 else 1
    one = pl.BlockSpec((group, tile, width), lambda i, *_: (i, 0, 0))
    grid_spec = pltpu.PrefetchScalarGridSpec(
        num_scalar_prefetch=3,
        grid=(n_q // group,),
        in_specs=[one] + [whole(x) for x in (kl, kc, kr, vl, vc, vr)],
        out_specs=one,
    )
    cost = pl.CostEstimate(
        flops=n_q * KEEP * tile * key_tile * width * 4,
        transcendentals=n_q * KEEP * tile * key_tile,
        bytes_accessed=2 * (q.size * 2 + (kl.size + kc.size + kr.size) * 2),
    )
    return pl.pallas_call(
        attend_kernel,
        grid_spec=grid_spec,
        out_shape=jax.ShapeDtypeStruct(q.shape, q.dtype),
        compiler_params=pltpu.CompilerParams(dimension_semantics=("arbitrary",)),
        cost_estimate=cost,
    )(which, index, count, q, kl, kc, kr, vl, vc, vr)


def body(query_rows, key_rows, value_rows, kept_tiles):
    key_local, value_local = (
        lax.all_to_all(key_rows, "uly", split_axis=1, concat_axis=0, tiled=True),
        lax.all_to_all(value_rows, "uly", split_axis=1, concat_axis=0, tiled=True),
    )
    n_uly = lax.axis_size("uly")
    n_blk = lax.axis_size("blk")
    feat_width = key_local.shape[1]
    slab_now = lax.axis_index("blk")
    rows = query_rows.shape[0]
    chunk = rows // CHUNKS

    from_left, from_right = run_starts(kept_tiles, n_blk, n_uly)
    key_tiles = jnp.swapaxes(key_local.reshape(n_uly, TILE, feat_width), 1, 2)
    value_tiles = value_local.reshape(n_uly, TILE, feat_width)

    to_next = from_left[jnp.minimum(slab_now + 1, n_blk - 1)]
    to_prev = from_right[jnp.maximum(slab_now - 1, 0)]
    run_next = (
        lax.dynamic_slice_in_dim(key_tiles, to_next, USED, 0),
        lax.dynamic_slice_in_dim(value_tiles, to_next, USED, 0),
    )
    run_prev = (
        lax.dynamic_slice_in_dim(key_tiles, to_prev, USED, 0),
        lax.dynamic_slice_in_dim(value_tiles, to_prev, USED, 0),
    )
    left_key, left_value = passed_along(run_next, "blk", 1)
    right_key, right_value = passed_along(run_prev, "blk", -1)

    position = jnp.arange(n_uly, dtype=jnp.int32)
    listed = jnp.take(kept_tiles, position * n_blk + slab_now, axis=0)
    is_live = listed >= 0
    safe = jnp.where(is_live, listed, 0)
    relative = safe % n_blk - slab_now
    tile_pos = safe // n_blk
    which = (relative + 1).astype(jnp.int32)
    index = jnp.where(
        relative == 0,
        tile_pos,
        jnp.where(relative < 0, tile_pos - from_left[slab_now], tile_pos - from_right[slab_now]),
    ).astype(jnp.int32)
    index = jnp.where(is_live, index, 0)
    which = jnp.where(is_live, which, 1)
    count = jnp.sum(is_live.astype(jnp.int32), axis=1)

    query_rows, left_key, right_key = lax.optimization_barrier((query_rows, left_key, right_key))
    pieces = []
    for c in range(CHUNKS):
        query_part = lax.all_to_all(
            query_rows[c * chunk:(c + 1) * chunk], "uly", split_axis=1, concat_axis=0, tiled=True
        ).reshape(n_uly, chunk, feat_width)
        attended = attend(
            which.reshape(-1), index.reshape(-1), count,
            query_part, left_key, key_tiles, right_key, left_value, value_tiles, right_value,
        )
        attended = attended.reshape(n_uly * chunk, feat_width)
        pieces.append(lax.all_to_all(attended, "uly", split_axis=0, concat_axis=1, tiled=True))
    return jnp.concatenate(pieces, axis=0)


def solution(mesh):
    placed = (P(("uly", "blk"), None), P(("uly", "blk"), None), P(("uly", "blk"), None), P())
    return jax.shard_map(
        body, mesh=mesh, in_specs=placed, out_specs=P(("uly", "blk"), None), check_vma=False
    )
```

```python
import functools

import jax
import jax.numpy as jnp
from jax import lax
from jax.experimental import pallas as pl
from jax.experimental.pallas import tpu as pltpu
from jax.sharding import PartitionSpec as P

HEAD_DIM = 128
TILE = 384
KEEP = 6
USED = 8
CHUNKS = 1
GROUP = 4
LOG2_E = 1.4426950408889634


def passed_along(block, axis, distance):
    devices = range(lax.axis_size(axis))
    route = [(i - distance, i) for i in devices if i - distance in devices]
    return lax.ppermute(block, axis, route)


def run_starts(kept_tiles, n_blk, slab_tiles):
    rows = kept_tiles.shape[0]
    row_slab = (jnp.arange(rows, dtype=jnp.int32) % n_blk)[:, None]
    live = kept_tiles >= 0
    entry_slab = jnp.where(live, kept_tiles % n_blk, -5)
    entry_pos = kept_tiles // n_blk
    slabs = jnp.arange(n_blk, dtype=jnp.int32)
    big = jnp.int32(slab_tiles + 1)

    def start_for(shift):
        hit = (row_slab[None] == slabs[:, None, None]) & (
            entry_slab[None] == slabs[:, None, None] + shift
        )
        low = jnp.min(jnp.where(hit, entry_pos[None], big), axis=(1, 2))
        return jnp.where(low == big, 0, jnp.minimum(low, slab_tiles - USED))

    return start_for(-1), start_for(1)


def attend_kernel(which_ref, index_ref, count_ref, q_ref, kl_ref, kc_ref, kr_ref,
                  vl_ref, vc_ref, vr_ref, o_ref):
    for g in range(q_ref.shape[0]):
        attend_one(g, pl.program_id(0) * q_ref.shape[0] + g, which_ref, index_ref, count_ref,
                   q_ref, kl_ref, kc_ref, kr_ref, vl_ref, vc_ref, vr_ref, o_ref)


def attend_one(g, i, which_ref, index_ref, count_ref, q_ref, kl_ref, kc_ref, kr_ref,
               vl_ref, vc_ref, vr_ref, o_ref):
    n = count_ref[i]
    score_scale = (HEAD_DIM ** (-0.5)) * LOG2_E
    q = q_ref[g]

    def pick(l_ref, c_ref, r_ref, j):
        w = which_ref[i * KEEP + j]
        x = index_ref[i * KEEP + j]
        side = l_ref.shape[0] - 1
        own = c_ref.shape[0] - 1
        a = l_ref[jnp.clip(x, 0, side)]
        b = c_ref[jnp.clip(x, 0, own)]
        c = r_ref[jnp.clip(x, 0, side)]
        return jnp.where(w == 0, a, jnp.where(w == 1, b, c))

    scores = []
    top = None
    for j in range(KEEP):
        s = jnp.dot(q, pick(kl_ref, kc_ref, kr_ref, j),
                    preferred_element_type=jnp.float32) * score_scale
        if j > 0:
            s = jnp.where(j < n, s, -jnp.inf)
        scores.append(s)
        top = s if top is None else jnp.maximum(top, s)
    m = jnp.max(top, axis=1, keepdims=True)

    spread = None
    acc = None
    for j in range(KEEP):
        p = jnp.exp2(scores[j] - m)
        pv = jnp.dot(p.astype(jnp.bfloat16), pick(vl_ref, vc_ref, vr_ref, j),
                     preferred_element_type=jnp.float32)
        spread = p if spread is None else spread + p
        acc = pv if acc is None else acc + pv
    total = jnp.sum(spread, axis=1, keepdims=True)
    o_ref[g] = (acc / total).astype(o_ref.dtype)


def attend(which, index, count, q, kl, kc, kr, vl, vc, vr):
    n_q, tile, width = q.shape
    key_tile = vc.shape[1]

    def whole(x):
        return pl.BlockSpec(x.shape, lambda i, *_: (0, 0, 0))

    group = GROUP if n_q % GROUP == 0 else 1
    one = pl.BlockSpec((group, tile, width), lambda i, *_: (i, 0, 0))
    grid_spec = pltpu.PrefetchScalarGridSpec(
        num_scalar_prefetch=3,
        grid=(n_q // group,),
        in_specs=[one] + [whole(x) for x in (kl, kc, kr, vl, vc, vr)],
        out_specs=one,
    )
    cost = pl.CostEstimate(
        flops=n_q * KEEP * tile * key_tile * width * 4,
        transcendentals=n_q * KEEP * tile * key_tile,
        bytes_accessed=2 * (q.size * 2 + (kl.size + kc.size + kr.size) * 2),
    )
    return pl.pallas_call(
        attend_kernel,
        grid_spec=grid_spec,
        out_shape=jax.ShapeDtypeStruct(q.shape, q.dtype),
        compiler_params=pltpu.CompilerParams(dimension_semantics=("arbitrary",)),
        cost_estimate=cost,
    )(which, index, count, q, kl, kc, kr, vl, vc, vr)


def body(query_rows, key_rows, value_rows, kept_tiles):
    key_local, value_local = (
        lax.all_to_all(key_rows, "uly", split_axis=1, concat_axis=0, tiled=True),
        lax.all_to_all(value_rows, "uly", split_axis=1, concat_axis=0, tiled=True),
    )
    n_uly = lax.axis_size("uly")
    n_blk = lax.axis_size("blk")
    feat_width = key_local.shape[1]
    slab_now = lax.axis_index("blk")
    rows = query_rows.shape[0]
    chunk = rows // CHUNKS

    from_left, from_right = run_starts(kept_tiles, n_blk, n_uly)
    key_tiles = jnp.swapaxes(key_local.reshape(n_uly, TILE, feat_width), 1, 2)
    value_tiles = value_local.reshape(n_uly, TILE, feat_width)

    to_next = from_left[jnp.minimum(slab_now + 1, n_blk - 1)]
    to_prev = from_right[jnp.maximum(slab_now - 1, 0)]
    run_next = (
        lax.dynamic_slice_in_dim(key_tiles, to_next, USED, 0),
        lax.dynamic_slice_in_dim(value_tiles, to_next, USED, 0),
    )
    run_prev = (
        lax.dynamic_slice_in_dim(key_tiles, to_prev, USED, 0),
        lax.dynamic_slice_in_dim(value_tiles, to_prev, USED, 0),
    )
    left_key, left_value = passed_along(run_next, "blk", 1)
    right_key, right_value = passed_along(run_prev, "blk", -1)

    position = jnp.arange(n_uly, dtype=jnp.int32)
    listed = jnp.take(kept_tiles, position * n_blk + slab_now, axis=0)
    is_live = listed >= 0
    safe = jnp.where(is_live, listed, 0)
    relative = safe % n_blk - slab_now
    tile_pos = safe // n_blk
    which = (relative + 1).astype(jnp.int32)
    index = jnp.where(
        relative == 0,
        tile_pos,
        jnp.where(relative < 0, tile_pos - from_left[slab_now], tile_pos - from_right[slab_now]),
    ).astype(jnp.int32)
    index = jnp.where(is_live, index, 0)
    which = jnp.where(is_live, which, 1)
    count = jnp.sum(is_live.astype(jnp.int32), axis=1)

    query_heads = jnp.transpose(query_rows.reshape(rows, n_uly, feat_width), (1, 0, 2))
    query_heads, left_key, right_key = lax.optimization_barrier((query_heads, left_key, right_key))
    pieces = []
    for c in range(CHUNKS):
        query_part = lax.all_to_all(
            query_heads[:, c * chunk:(c + 1) * chunk], "uly", split_axis=0, concat_axis=0, tiled=True
        )
        attended = attend(
            which.reshape(-1), index.reshape(-1), count,
            query_part, left_key, key_tiles, right_key, left_value, value_tiles, right_value,
        )
        attended = attended.reshape(n_uly * chunk, feat_width)
        pieces.append(lax.all_to_all(attended, "uly", split_axis=0, concat_axis=1, tiled=True))
    return jnp.concatenate(pieces, axis=0)


def solution(mesh):
    placed = (P(("uly", "blk"), None), P(("uly", "blk"), None), P(("uly", "blk"), None), P())
    return jax.shard_map(
        body, mesh=mesh, in_specs=placed, out_specs=P(("uly", "blk"), None), check_vma=False
    )
```
